1024 devices in a mesh: expert: 32 (over z), dp: 32 (over y, x, core).
Axes of the slice: x: 4, y: 4, z: 32, core: 2. Of those that a mesh axis runs over, the one named last changes fastest.
Arguments:
- grad_out: bfloat16 [8192, 7168], P(('expert', 'dp')), may hold values from -6 to 6
- combine: bfloat16 [8192, 8], P(('expert', 'dp')), may hold values from 0.019897461 to 0.29882812
- expert_ids: int32 [8192, 8], P(('expert', 'dp')), may hold values from 0 to 127, as said below
- saved_hidden: bfloat16 [32, 32, 32, 3, 1024], P('expert', 'dp'), may hold values from -6 to 6
Outputs:
- grad_down: bfloat16 [128, 1024, 7168], P('expert', None, 'dp')
The draws below stay inside these ranges and needn't reach their ends.
Inputs may be any that keep to these rules, and one draw needn't show every extreme that they name: `expert_ids`: within the 64 entries of one device (an aligned block of 8 tokens), each destination index id // 4 is named at most 3 times, and some destination exactly 3 times; over the devices of one data group every destination is named exactly 8 * 8 times. `saved_hidden`: rows of slots that no entry names hold arbitrary values.
All inputs are finite; a program needn't handle non-finite values.
Results may differ from the reference program's by a relative error of at most 0.0049.
Values may be sent and summed in bfloat16 or wider, within the bound.
No kernel may reach another device: no remote copies, remote signals or barrier semaphores. Data moves between devices by JAX's collectives and lax.ppermute only.
A program may use at most 32 MiB of HBM per device.

```python
import jax
import jax.numpy as jnp
from jax import lax

D = 7168
FF = 1024
TOP = 8
EXP_DEV = 4
TOK_DEV = 8
EXPERTS = 128
CAP = 3
TOKENS = 8192
N_EXPERT = 32
N_DP = 32


def draw_expert_ids(key, part):
    per_block = TOK_DEV * TOP
    base_count = per_block // N_EXPERT
    slot_total = N_EXPERT * CAP
    keys = jax.random.split(key, 4)
    firsts = jax.vmap(lambda k: jax.random.permutation(k, N_EXPERT))(jax.random.split(keys[0], N_DP)).astype(jnp.int32)
    shifts = jax.random.randint(keys[1], (N_DP,), 1, N_EXPERT).astype(jnp.int32)
    sources = jnp.arange(N_EXPERT, dtype=jnp.int32)
    seconds = jnp.take_along_axis(firsts, (sources[None, :] + shifts[:, None]) % N_EXPERT, axis=1)
    targets = jnp.arange(N_EXPERT, dtype=jnp.int32)
    counts = base_count + (targets[None, None, :] == firsts[:, :, None]).astype(jnp.int32) - (targets[None, None, :] == seconds[:, :, None]).astype(jnp.int32)
    places = jnp.arange(CAP, dtype=jnp.int32)
    live_slots = (places[None, None, None, :] < counts[:, :, :, None]).reshape(N_DP, N_EXPERT, slot_total)
    orders = jax.vmap(lambda k: jax.random.permutation(k, slot_total))(jax.random.split(keys[2], N_DP * N_EXPERT)).reshape(N_DP, N_EXPERT, slot_total).astype(jnp.int32)
    scores = orders + (1 - live_slots.astype(jnp.int32)) * slot_total
    chosen = jnp.argsort(scores, axis=2, stable=True)[:, :, :per_block].astype(jnp.int32)
    target_of = chosen // CAP
    place_of = chosen % CAP
    offsets = jax.random.randint(keys[3], (N_DP, N_EXPERT, N_EXPERT), 0, EXP_DEV).astype(jnp.int32)
    first_local = jnp.take_along_axis(offsets, target_of, axis=2)
    local_expert = (first_local + place_of) % EXP_DEV
    chosen_ids = target_of * EXP_DEV + local_expert
    chosen_ids = jnp.transpose(chosen_ids, (1, 0, 2)).reshape(N_EXPERT * N_DP * TOK_DEV, TOP)
    return chosen_ids.astype(jnp.int32)


def level_of(rng, shape, pieces, low, top_value):
    loudness = 1.0
    for position, parts in pieces:
        heights = jax.random.uniform(jax.random.fold_in(jax.random.fold_in(rng, 6), position), (parts,), jnp.float32, low / len(pieces), top_value / len(pieces))
        loudness = loudness * jnp.repeat(jnp.exp(heights), shape[position] // parts).reshape((-1,) + (1,) * (len(shape) - 1 - position))
    return loudness


def normal_values(own_key, extent, spread, limit, pieces=(), kind=jnp.bfloat16):
    values = jax.random.normal(own_key, extent, jnp.float32) * spread
    if len(pieces) > 0:
        values = level_of(own_key, extent, pieces, -0.22, 0.18) * values
    return jnp.clip(values, min=-limit, max=limit).astype(kind)


def setup_inputs(seed: int = 0) -> dict:
    seeds = jax.random.split(jax.random.key(seed), 5)
    return {
        "grad_out": normal_values(seeds[0], (TOKENS, D), 1.0, 6.0, ((0, 1024),)),
        "combine": jnp.clip(0.019897461 + 0.27893066 * jax.random.uniform(seeds[1], (TOKENS, TOP), jnp.float32) ** level_of(seeds[1], (TOKENS, TOP), ((0, 1024),), -0.2, 0.2), 0.019897461, 0.29882812).astype(jnp.bfloat16),
        "expert_ids": draw_expert_ids(jax.random.fold_in(seeds[4], 71), 0),
        "saved_hidden": normal_values(seeds[3], (N_EXPERT, N_DP, N_EXPERT, CAP, FF), 1.0, 6.0, ((0, 32), (1, 32))),
    }


def reference(grad_out, combine, expert_ids, saved_hidden):
    entries = TOKENS * TOP
    per_block = TOK_DEV * TOP
    destination = (expert_ids // EXP_DEV).reshape(-1).astype(jnp.int32)
    local_expert = (expert_ids % EXP_DEV).reshape(-1).astype(jnp.int32)
    blocked = destination.reshape(entries // per_block, per_block)
    onehot = (blocked[:, :, None] == jnp.arange(N_EXPERT, dtype=jnp.int32)[None, None, :]).astype(jnp.int32)
    before = jnp.cumsum(onehot, axis=1) - onehot
    slot_rank = jnp.sum(before * onehot, axis=2).reshape(-1).astype(jnp.int32)
    block_of = jnp.arange(entries, dtype=jnp.int32) // per_block
    source = block_of // N_DP
    group_index = block_of % N_DP
    slot_index = (((destination * N_DP + group_index) * N_EXPERT + source) * CAP + slot_rank).astype(jnp.int32)
    hidden_flat = saved_hidden.reshape(-1, FF)
    weight_flat = combine.reshape(-1)
    by_destination = jnp.argsort(destination, stable=True).astype(jnp.int32).reshape(N_EXPERT, entries // N_EXPERT)

    def one_destination(entry_rows):
        hidden_rows = hidden_flat[slot_index[entry_rows]]
        weighted = (weight_flat[entry_rows].astype(jnp.float32)[:, None] * hidden_rows.astype(jnp.float32)).astype(jnp.bfloat16)
        grad_rows = grad_out[entry_rows // TOP]
        owners = local_expert[entry_rows]

        def one_expert(expert_index):
            masked = jnp.where((owners == expert_index)[:, None], weighted, jnp.zeros_like(weighted))
            return lax.dot_general(masked, grad_rows, (((0,), (0,)), ((), ())), preferred_element_type=jnp.float32).astype(jnp.bfloat16)

        return lax.map(one_expert, jnp.arange(EXP_DEV, dtype=jnp.int32))

    result = lax.map(one_destination, by_destination)
    return result.reshape(EXPERTS, FF, D)
```

```python
import jax
import jax.numpy as jnp
from jax import lax
from jax.sharding import PartitionSpec as P

D = 7168
FF = 1024
TOP = 8
EXP_DEV = 4
TOK_DEV = 8


def slot_tables(meta_all, me_exp, me_grp, capacity):
    n_src = meta_all.shape[0]
    per_block = TOK_DEV * TOP
    ids = meta_all[:, :, :TOP].astype(jnp.int32).reshape(n_src, per_block)
    wts = meta_all[:, :, TOP:].reshape(n_src, per_block)
    n_dest = lax.axis_size("expert")
    destination = ids // EXP_DEV
    local = ids % EXP_DEV
    onehot = (destination[:, :, None] == jnp.arange(n_dest, dtype=jnp.int32)[None, None, :]).astype(
        jnp.int32
    )
    before = jnp.cumsum(onehot, axis=1) - onehot
    rank = jnp.sum(before * onehot, axis=2)
    mine = destination == me_exp
    select = mine[:, None, :] & (
        rank[:, None, :] == jnp.arange(capacity, dtype=jnp.int32)[None, :, None]
    )
    weight = jnp.sum(jnp.where(select, wts[:, None, :], 0.0), axis=2)
    label = jnp.sum(jnp.where(select, local[:, None, :], 0), axis=2)
    token_in_block = jnp.arange(per_block, dtype=jnp.int32) // TOP
    token = jnp.sum(jnp.where(select, token_in_block[None, None, :], 0), axis=2)
    block = jnp.arange(n_src, dtype=jnp.int32) * lax.axis_size("dp") + me_grp
    token = token + block[:, None] * TOK_DEV
    live = jnp.any(select, axis=2)
    return weight.reshape(-1), label.reshape(-1), token.reshape(-1), live.reshape(-1)


def per_device(grad_out, combine, expert_ids, saved_hidden):
    n_grp = lax.axis_size("dp")
    capacity = saved_hidden.shape[3]
    width = D // n_grp
    live_count = TOK_DEV * TOP
    me_exp = lax.axis_index("expert")
    me_grp = lax.axis_index("dp")

    cols = jnp.transpose(grad_out.reshape(TOK_DEV, n_grp, width), (1, 0, 2))
    cols = lax.all_to_all(cols, "dp", 0, 0, tiled=True)
    tokens = lax.all_gather(cols, "expert", axis=0, tiled=False).reshape(-1, width)

    meta = jnp.concatenate(
        [expert_ids.astype(jnp.float32), combine.astype(jnp.float32)], axis=1
    )
    meta_all = lax.all_gather(meta, "expert", axis=0, tiled=False)
    weight, label, token, live = slot_tables(meta_all, me_exp, me_grp, capacity)

    hidden = saved_hidden.reshape(-1, FF)
    weighted = (weight[:, None] * hidden.astype(jnp.float32)).astype(jnp.bfloat16)
    position = jnp.cumsum(live.astype(jnp.int32)) - 1
    pick = live[None, :] & (position[None, :] == jnp.arange(live_count, dtype=jnp.int32)[:, None])
    packed = jnp.dot(
        pick.astype(jnp.bfloat16), weighted, preferred_element_type=jnp.float32
    ).astype(jnp.bfloat16)
    label_c = jnp.sum(jnp.where(pick, label[None, :], 0), axis=1)
    token_c = jnp.sum(jnp.where(pick, token[None, :], 0), axis=1)
    extra = jnp.stack([label_c, token_c // 128, token_c % 128], axis=1).astype(jnp.bfloat16)
    extra = jnp.pad(extra, ((0, 0), (0, 128 - extra.shape[1])))
    payload = jnp.concatenate([packed, extra], axis=1)
    gathered = lax.all_gather(payload, "dp", axis=0, tiled=True)

    rows = gathered[:, :FF]
    labels = gathered[:, FF].astype(jnp.int32)
    picks = gathered[:, FF + 1].astype(jnp.int32) * 128 + gathered[:, FF + 2].astype(jnp.int32)
    grad_rows = jnp.take(tokens, picks, axis=0, mode="clip")
    mask = labels[:, None] == jnp.arange(EXP_DEV, dtype=jnp.int32)[None, :]
    spread = jnp.where(mask[:, :, None], rows[:, None, :], jnp.zeros_like(rows)[:, None, :])
    spread = spread.reshape(rows.shape[0], EXP_DEV * FF)
    gradient = lax.dot_general(
        spread, grad_rows, (((0,), (0,)), ((), ())), preferred_element_type=jnp.float32
    )
    return gradient.reshape(EXP_DEV, FF, width).astype(jnp.bfloat16)


def solution(mesh):
    placed = (
        P(("expert", "dp"), None),
        P(("expert", "dp"), None),
        P(("expert", "dp"), None),
        P("expert", "dp", None, None, None),
    )
    return jax.shard_map(
        per_device, mesh=mesh, in_specs=placed, out_specs=P("expert", None, "dp"), check_vma=False
    )
```

```python
import jax
import jax.numpy as jnp
from jax import lax
from jax.sharding import PartitionSpec as P

D = 7168
FF = 1024
TOP = 8
EXP_DEV = 4
TOK_DEV = 8


def slot_tables(meta_all, me_exp, me_grp, capacity, chunks):
    n_src = meta_all.shape[0]
    per_block = TOK_DEV * TOP
    ids = meta_all[:, :, :TOP].astype(jnp.int32).reshape(n_src, per_block)
    wts = meta_all[:, :, TOP:].astype(jnp.float32).reshape(n_src, per_block)
    n_dest = lax.axis_size("expert")
    destination = ids // EXP_DEV
    local = ids % EXP_DEV
    onehot = (destination[:, :, None] == jnp.arange(n_dest, dtype=jnp.int32)[None, None, :]).astype(
        jnp.int32
    )
    before = jnp.cumsum(onehot, axis=1) - onehot
    rank = jnp.sum(before * onehot, axis=2)
    mine = destination == me_exp
    select = mine[:, None, :] & (
        rank[:, None, :] == jnp.arange(capacity, dtype=jnp.int32)[None, :, None]
    )
    weight = jnp.sum(jnp.where(select, wts[:, None, :], 0.0), axis=2)
    label = jnp.sum(jnp.where(select, local[:, None, :], 0), axis=2)
    token_in_block = jnp.arange(per_block, dtype=jnp.int32) // TOP
    token = jnp.sum(jnp.where(select, token_in_block[None, None, :], 0), axis=2)
    block = jnp.arange(n_src, dtype=jnp.int32) * chunks + me_grp
    token = token + block[:, None] * TOK_DEV
    live = jnp.any(select, axis=2)
    return weight.reshape(-1), label.reshape(-1), token.reshape(-1), live.reshape(-1)


def per_device(grad_out, combine, expert_ids, saved_hidden):
    n_grp = lax.axis_size("dp")
    capacity = saved_hidden.shape[3]
    width = D // n_grp
    live_count = TOK_DEV * TOP
    me_exp = lax.axis_index("expert")
    me_grp = lax.axis_index("dp")

    cols = jnp.transpose(grad_out.reshape(TOK_DEV, n_grp, width), (1, 0, 2))
    cols = lax.all_to_all(cols, "dp", 0, 0, tiled=True)
    meta = jnp.concatenate([expert_ids.astype(jnp.bfloat16), combine], axis=1)
    meta = jnp.pad(meta, ((0, 0), (0, width - meta.shape[1])))[None]
    chunks = n_grp + 1
    everything = lax.all_gather(
        jnp.concatenate([cols, meta], axis=0), "expert", axis=0, tiled=False
    )
    tokens = everything.reshape(-1, width)
    meta_all = everything[:, n_grp, :, : 2 * TOP]
    weight, label, token, live = slot_tables(meta_all, me_exp, me_grp, capacity, chunks)

    hidden = saved_hidden.reshape(-1, FF)
    weighted = (weight[:, None] * hidden.astype(jnp.float32)).astype(jnp.bfloat16)
    position = jnp.cumsum(live.astype(jnp.int32)) - 1
    pick = live[None, :] & (position[None, :] == jnp.arange(live_count, dtype=jnp.int32)[:, None])
    packed = jnp.dot(
        pick.astype(jnp.bfloat16), weighted, preferred_element_type=jnp.float32
    ).astype(jnp.bfloat16)
    label_c = jnp.sum(jnp.where(pick, label[None, :], 0), axis=1)
    token_c = jnp.sum(jnp.where(pick, token[None, :], 0), axis=1)
    extra = jnp.stack([label_c, token_c // 128, token_c % 128], axis=1).astype(jnp.bfloat16)
    extra = jnp.pad(extra, ((0, 0), (0, 128 - extra.shape[1])))
    payload = jnp.concatenate([packed, extra], axis=1)
    gathered = lax.all_gather(payload, "dp", axis=0, tiled=True)

    rows = gathered[:, :FF]
    labels = gathered[:, FF].astype(jnp.int32)
    picks = gathered[:, FF + 1].astype(jnp.int32) * 128 + gathered[:, FF + 2].astype(jnp.int32)
    grad_rows = jnp.take(tokens, picks, axis=0, mode="clip")
    mask = labels[:, None] == jnp.arange(EXP_DEV, dtype=jnp.int32)[None, :]
    spread = jnp.where(mask[:, :, None], rows[:, None, :], jnp.zeros_like(rows)[:, None, :])
    spread = spread.reshape(rows.shape[0], EXP_DEV * FF)
    gradient = lax.dot_general(
        spread, grad_rows, (((0,), (0,)), ((), ())), preferred_element_type=jnp.float32
    )
    return gradient.reshape(EXP_DEV, FF, width).astype(jnp.bfloat16)


def solution(mesh):
    placed = (
        P(("expert", "dp"), None),
        P(("expert", "dp"), None),
        P(("expert", "dp"), None),
        P("expert", "dp", None, None, None),
    )
    return jax.shard_map(
        per_device, mesh=mesh, in_specs=placed, out_specs=P("expert", None, "dp"), check_vma=False
    )
```

```python
import jax
import jax.numpy as jnp
from jax import lax
from jax.sharding import PartitionSpec as P

D = 7168
FF = 1024
TOP = 8
EXP_DEV = 4
TOK_DEV = 8


def slot_tables(meta_gs, me_exp, relative, capacity):
    n_grp, n_src = meta_gs.shape[:2]
    per_block = TOK_DEV * TOP
    ids = meta_gs[..., :TOP].astype(jnp.int32).reshape(n_grp, n_src, per_block)
    wts = meta_gs[..., TOP:].astype(jnp.float32).reshape(n_grp, n_src, per_block)
    destination = ids // EXP_DEV
    local = ids % EXP_DEV
    entry = jnp.arange(per_block, dtype=jnp.int32)
    earlier = entry[None, :] < entry[:, None]
    same = destination[..., :, None] == destination[..., None, :]
    rank = jnp.sum((same & earlier).astype(jnp.int32), axis=-1)
    mine = destination == me_exp
    select = mine[:, :, None, :] & (
        rank[:, :, None, :] == jnp.arange(capacity, dtype=jnp.int32)[None, None, :, None]
    )
    weight = jnp.sum(jnp.where(select, wts[:, :, None, :], 0.0), axis=-1)
    label = jnp.sum(jnp.where(select, local[:, :, None, :] + 1, 0), axis=-1) - 1
    token_in_block = jnp.sum(jnp.where(select, (entry // TOP)[None, None, None, :], 0), axis=-1)
    block = relative[None, :] * n_grp + jnp.arange(n_grp, dtype=jnp.int32)[:, None]
    token = token_in_block + block[:, :, None] * TOK_DEV
    return weight.reshape(-1), label.reshape(-1), token.reshape(-1)


def per_device(grad_out, combine, expert_ids, saved_hidden):
    n_exp = lax.axis_size("expert")
    n_grp = lax.axis_size("dp")
    capacity = saved_hidden.shape[3]
    width = D // n_grp
    me_exp = lax.axis_index("expert")

    hidden = lax.all_gather(saved_hidden.reshape(-1, FF), "dp", axis=0, tiled=True)

    meta = jnp.concatenate([expert_ids.astype(jnp.bfloat16), combine], axis=1)
    cols = jnp.transpose(grad_out.reshape(TOK_DEV, n_grp, width), (1, 0, 2))
    cols = jnp.concatenate(
        [cols, jnp.broadcast_to(meta[None], (n_grp,) + meta.shape)], axis=2
    )
    cols = lax.all_to_all(cols, "dp", 0, 0, tiled=True)

    half = n_exp // 2
    fwd_perm = [(i, (i + 1) % n_exp) for i in range(n_exp)]
    bwd_perm = [(i, (i - 1) % n_exp) for i in range(n_exp)]
    ahead = [cols]
    behind = []
    fwd = cols
    bwd = cols
    for step in range(1, half + 1):
        fwd = lax.ppermute(fwd, "expert", fwd_perm)
        behind.append(fwd)
        if step < n_exp - half:
            bwd = lax.ppermute(bwd, "expert", bwd_perm)
            ahead.append(bwd)
    ring = jnp.stack(ahead + behind[::-1], axis=0)
    tokens = ring.reshape(-1, ring.shape[-1])

    relative = (jnp.arange(n_exp, dtype=jnp.int32) - me_exp) % n_exp
    meta_src = jnp.take(ring[:, :, :, width:], relative, axis=0)
    meta_gs = jnp.transpose(meta_src, (1, 0, 2, 3))
    weight, label, token = slot_tables(meta_gs, me_exp, relative, capacity)

    rows = (weight[:, None] * hidden.astype(jnp.float32)).astype(jnp.bfloat16)
    grad_rows = jnp.take(tokens, token, axis=0, mode="clip")[:, :width]
    mask = label[:, None] == jnp.arange(EXP_DEV, dtype=jnp.int32)[None, :]
    spread = jnp.where(mask[:, :, None], rows[:, None, :], jnp.zeros_like(rows)[:, None, :])
    spread = spread.reshape(rows.shape[0], EXP_DEV * FF)
    gradient = lax.dot_general(
        spread, grad_rows, (((0,), (0,)), ((), ())), preferred_element_type=jnp.float32
    )
    return gradient.reshape(EXP_DEV, FF, width).astype(jnp.bfloat16)


def solution(mesh):
    placed = (
        P(("expert", "dp"), None),
        P(("expert", "dp"), None),
        P(("expert", "dp"), None),
        P("expert", "dp", None, None, None),
    )
    return jax.shard_map(
        per_device, mesh=mesh, in_specs=placed, out_specs=P("expert", None, "dp"), check_vma=False
    )
```

```python
import jax
import jax.numpy as jnp
from jax import lax
from jax.sharding import PartitionSpec as P

D = 7168
FF = 1024
TOP = 8
EXP_DEV = 4
TOK_DEV = 8


def slot_tables(meta_gs, me_exp, relative, capacity):
    n_grp, n_src = meta_gs.shape[:2]
    per_block = TOK_DEV * TOP
    ids = meta_gs[..., :TOP].astype(jnp.int32).reshape(n_grp, n_src, per_block)
    wts = meta_gs[..., TOP:].astype(jnp.float32).reshape(n_grp, n_src, per_block)
    destination = ids // EXP_DEV
    local = ids % EXP_DEV
    entry = jnp.arange(per_block, dtype=jnp.int32)
    mine = destination == me_exp
    rank = jnp.cumsum(mine.astype(jnp.int32), axis=-1) - mine.astype(jnp.int32)
    select = mine[:, :, None, :] & (
        rank[:, :, None, :] == jnp.arange(capacity, dtype=jnp.int32)[None, None, :, None]
    )
    weight = jnp.sum(jnp.where(select, wts[:, :, None, :], 0.0), axis=-1)
    label = jnp.sum(jnp.where(select, local[:, :, None, :] + 1, 0), axis=-1) - 1
    token_in_block = jnp.sum(jnp.where(select, (entry // TOP)[None, None, None, :], 0), axis=-1)
    block = relative[None, :] * n_grp + jnp.arange(n_grp, dtype=jnp.int32)[:, None]
    token = token_in_block + block[:, :, None] * TOK_DEV
    return weight.reshape(-1), label.reshape(-1), token.reshape(-1)


def per_device(grad_out, combine, expert_ids, saved_hidden):
    n_exp = lax.axis_size("expert")
    n_grp = lax.axis_size("dp")
    capacity = saved_hidden.shape[3]
    width = D // n_grp
    me_exp = lax.axis_index("expert")

    hidden = lax.all_gather(saved_hidden.reshape(-1, FF), "dp", axis=0, tiled=True)

    meta = jnp.concatenate([expert_ids.astype(jnp.bfloat16), combine], axis=1)
    cols = jnp.transpose(grad_out.reshape(TOK_DEV, n_grp, width), (1, 0, 2))
    cols = jnp.concatenate(
        [cols, jnp.broadcast_to(meta[None], (n_grp,) + meta.shape)], axis=2
    )
    cols = lax.all_to_all(cols, "dp", 0, 0, tiled=True)

    half = n_exp // 2
    fwd_perm = [(i, (i + 1) % n_exp) for i in range(n_exp)]
    bwd_perm = [(i, (i - 1) % n_exp) for i in range(n_exp)]
    ahead = [cols]
    behind = []
    fwd = cols
    bwd = cols
    for step in range(1, half + 1):
        fwd = lax.ppermute(fwd, "expert", fwd_perm)
        behind.append(fwd)
        if step < n_exp - half:
            bwd = lax.ppermute(bwd, "expert", bwd_perm)
            ahead.append(bwd)
    ring = jnp.stack(ahead + behind[::-1], axis=0)
    tokens = ring.reshape(-1, ring.shape[-1])

    relative = (jnp.arange(n_exp, dtype=jnp.int32) - me_exp) % n_exp
    meta_src = jnp.take(ring[:, :, :, width:], relative, axis=0)
    meta_gs = jnp.transpose(meta_src, (1, 0, 2, 3))
    weight, label, token = slot_tables(meta_gs, me_exp, relative, capacity)

    rows = (weight[:, None] * hidden.astype(jnp.float32)).astype(jnp.bfloat16)
    grad_rows = jnp.take(tokens, token, axis=0, mode="clip")[:, :width]
    mask = label[:, None] == jnp.arange(EXP_DEV, dtype=jnp.int32)[None, :]
    spread = jnp.where(mask[:, :, None], rows[:, None, :], jnp.zeros_like(rows)[:, None, :])
    spread = spread.reshape(rows.shape[0], EXP_DEV * FF)
    gradient = lax.dot_general(
        spread, grad_rows, (((0,), (0,)), ((), ())), preferred_element_type=jnp.float32
    )
    return gradient.reshape(EXP_DEV, FF, width).astype(jnp.bfloat16)


def solution(mesh):
    placed = (
        P(("expert", "dp"), None),
        P(("expert", "dp"), None),
        P(("expert", "dp"), None),
        P("expert", "dp", None, None, None),
    )
    return jax.shard_map(
        per_device, mesh=mesh, in_specs=placed, out_specs=P("expert", None, "dp"), check_vma=False
    )
```

```python
import jax
import jax.numpy as jnp
from jax import lax
from jax.sharding import PartitionSpec as P

D = 7168
FF = 1024
TOP = 8
EXP_DEV = 4
TOK_DEV = 8


def chunk_tables(meta, me_exp, capacity):
    n_grp = meta.shape[0]
    per_block = TOK_DEV * TOP
    ids = meta[..., :TOP].astype(jnp.int32).reshape(n_grp, per_block)
    wts = meta[..., TOP:].astype(jnp.float32).reshape(n_grp, per_block)
    destination = ids // EXP_DEV
    local = ids % EXP_DEV
    entry = jnp.arange(per_block, dtype=jnp.int32)
    mine = destination == me_exp
    rank = jnp.cumsum(mine.astype(jnp.int32), axis=-1) - mine.astype(jnp.int32)
    select = mine[:, None, :] & (
        rank[:, None, :] == jnp.arange(capacity, dtype=jnp.int32)[None, :, None]
    )
    weight = jnp.sum(jnp.where(select, wts[:, None, :], 0.0), axis=-1)
    label = jnp.sum(jnp.where(select, local[:, None, :] + 1, 0), axis=-1) - 1
    token = jnp.sum(jnp.where(select, (entry // TOP)[None, None, :], 0), axis=-1)
    token = token + jnp.arange(n_grp, dtype=jnp.int32)[:, None] * TOK_DEV
    return weight, label, token


def per_device(grad_out, combine, expert_ids, saved_hidden):
    n_exp = lax.axis_size("expert")
    n_grp = lax.axis_size("dp")
    capacity = saved_hidden.shape[3]
    width = D // n_grp
    me_exp = lax.axis_index("expert")

    relative = (jnp.arange(n_exp, dtype=jnp.int32) + me_exp) % n_exp
    local_hidden = jnp.take(saved_hidden.reshape(n_exp, capacity, FF), relative, axis=0)
    hidden = lax.all_gather(local_hidden, "dp", axis=0, tiled=False)

    meta = jnp.concatenate([expert_ids.astype(jnp.bfloat16), combine], axis=1)
    cols = jnp.transpose(grad_out.reshape(TOK_DEV, n_grp, width), (1, 0, 2))
    cols = jnp.concatenate(
        [cols, jnp.broadcast_to(meta[None], (n_grp,) + meta.shape)], axis=2
    )
    cols = lax.all_to_all(cols, "dp", 0, 0, tiled=True)

    experts = jnp.arange(EXP_DEV, dtype=jnp.int32)

    def consume(chunk, r):
        weight, label, token = chunk_tables(chunk[:, :, width:], me_exp, capacity)
        rows = jnp.take(chunk.reshape(-1, chunk.shape[-1]), token, axis=0)[:, :, :width]
        mask = label[:, :, None] == experts[None, None, :]
        spread = jnp.where(mask[..., None], rows[:, :, None, :], jnp.zeros_like(rows)[:, :, None, :])
        spread = spread.reshape(rows.shape[0], rows.shape[1], EXP_DEV * width)
        scaled = (weight[:, :, None] * hidden[:, r].astype(jnp.float32)).astype(jnp.bfloat16)
        return spread, scaled

    half = n_exp // 2
    fwd_perm = [(i, (i + 1) % n_exp) for i in range(n_exp)]
    bwd_perm = [(i, (i - 1) % n_exp) for i in range(n_exp)]
    done = {0: consume(cols, 0)}
    fwd = cols
    bwd = cols
    for step in range(1, half + 1):
        fwd = lax.ppermute(fwd, "expert", fwd_perm)
        done[n_exp - step] = consume(fwd, n_exp - step)
        if step < n_exp - half:
            bwd = lax.ppermute(bwd, "expert", bwd_perm)
            done[step] = consume(bwd, step)
    spread = jnp.stack([done[r][0] for r in range(n_exp)], axis=0)
    scaled = jnp.stack([done[r][1] for r in range(n_exp)], axis=0)
    spread = spread.reshape(-1, EXP_DEV * width)
    scaled = scaled.reshape(-1, FF)
    gradient = lax.dot_general(
        scaled, spread, (((0,), (0,)), ((), ())), preferred_element_type=jnp.float32
    )
    gradient = gradient.astype(jnp.bfloat16).reshape(FF, EXP_DEV, width)
    return jnp.transpose(gradient, (1, 0, 2))


def solution(mesh):
    placed = (
        P(("expert", "dp"), None),
        P(("expert", "dp"), None),
        P(("expert", "dp"), None),
        P("expert", "dp", None, None, None),
    )
    return jax.shard_map(
        per_device, mesh=mesh, in_specs=placed, out_specs=P("expert", None, "dp"), check_vma=False
    )
```

```python
import jax
import jax.numpy as jnp
from jax import lax
from jax.sharding import PartitionSpec as P

D = 7168
FF = 1024
TOP = 8
EXP_DEV = 4
TOK_DEV = 8


def slot_tables(meta_gs, me_exp, relative, capacity):
    n_grp, n_src = meta_gs.shape[:2]
    per_block = TOK_DEV * TOP
    ids = meta_gs[..., :TOP].astype(jnp.int32).reshape(n_grp, n_src, per_block)
    wts = meta_gs[..., TOP:].astype(jnp.float32).reshape(n_grp, n_src, per_block)
    destination = ids // EXP_DEV
    local = ids % EXP_DEV
    entry = jnp.arange(per_block, dtype=jnp.int32)
    mine = destination == me_exp
    upper = (entry[:, None] < entry[None, :]).astype(jnp.bfloat16)
    rank = jnp.dot(
        mine.astype(jnp.bfloat16).reshape(-1, per_block), upper, preferred_element_type=jnp.float32
    )
    rank = rank.astype(jnp.int32).reshape(mine.shape)
    select = mine[:, :, None, :] & (
        rank[:, :, None, :] == jnp.arange(capacity, dtype=jnp.int32)[None, None, :, None]
    )
    weight = jnp.sum(jnp.where(select, wts[:, :, None, :], 0.0), axis=-1)
    label = jnp.sum(jnp.where(select, local[:, :, None, :] + 1, 0), axis=-1) - 1
    token_in_block = jnp.sum(jnp.where(select, (entry // TOP)[None, None, None, :], 0), axis=-1)
    block = relative[None, :] * n_grp + jnp.arange(n_grp, dtype=jnp.int32)[:, None]
    token = token_in_block + block[:, :, None] * TOK_DEV
    return weight.reshape(-1), label.reshape(-1), token.reshape(-1)


def per_device(grad_out, combine, expert_ids, saved_hidden):
    n_exp = lax.axis_size("expert")
    n_grp = lax.axis_size("dp")
    capacity = saved_hidden.shape[3]
    width = D // n_grp
    me_exp = lax.axis_index("expert")

    hidden = lax.all_gather(saved_hidden.reshape(-1, FF), "dp", axis=0, tiled=True)

    meta = jnp.concatenate([expert_ids.astype(jnp.bfloat16), combine], axis=1)
    cols = jnp.transpose(grad_out.reshape(TOK_DEV, n_grp, width), (1, 0, 2))
    cols = jnp.concatenate(
        [cols, jnp.broadcast_to(meta[None], (n_grp,) + meta.shape)], axis=2
    )
    cols = lax.all_to_all(cols, "dp", 0, 0, tiled=True)

    half = n_exp // 2
    fwd_perm = [(i, (i + 1) % n_exp) for i in range(n_exp)]
    bwd_perm = [(i, (i - 1) % n_exp) for i in range(n_exp)]
    ahead = [cols]
    behind = []
    fwd = cols
    bwd = cols
    for step in range(1, half + 1):
        fwd = lax.ppermute(fwd, "expert", fwd_perm)
        behind.append(fwd)
        if step < n_exp - half:
            bwd = lax.ppermute(bwd, "expert", bwd_perm)
            ahead.append(bwd)
    ring = jnp.stack(ahead + behind[::-1], axis=0)
    tokens = ring.reshape(-1, ring.shape[-1])

    relative = (jnp.arange(n_exp, dtype=jnp.int32) - me_exp) % n_exp
    meta_src = jnp.take(ring[:, :, :, width:], relative, axis=0)
    meta_gs = jnp.transpose(meta_src, (1, 0, 2, 3))
    weight, label, token = slot_tables(meta_gs, me_exp, relative, capacity)

    hidden_t = jnp.transpose(hidden)
    rows_t = (weight[None, :] * hidden_t.astype(jnp.float32)).astype(jnp.bfloat16)
    grad_rows = jnp.take(tokens, token, axis=0, mode="clip")[:, :width]
    mask = label[:, None] == jnp.arange(EXP_DEV, dtype=jnp.int32)[None, :]
    spread = jnp.where(mask[:, :, None], grad_rows[:, None, :], jnp.zeros_like(grad_rows)[:, None, :])
    spread = spread.reshape(grad_rows.shape[0], EXP_DEV * width)
    gradient = jnp.dot(rows_t, spread, preferred_element_type=jnp.float32)
    gradient = gradient.astype(jnp.bfloat16).reshape(FF, EXP_DEV, width)
    return jnp.transpose(gradient, (1, 0, 2))


def solution(mesh):
    placed = (
        P(("expert", "dp"), None),
        P(("expert", "dp"), None),
        P(("expert", "dp"), None),
        P("expert", "dp", None, None, None),
    )
    return jax.shard_map(
        per_device, mesh=mesh, in_specs=placed, out_specs=P("expert", None, "dp"), check_vma=False
    )
```

```python
import jax
import jax.numpy as jnp
from jax import lax
from jax.sharding import PartitionSpec as P

D = 7168
FF = 1024
TOP = 8
EXP_DEV = 4
TOK_DEV = 8


def slot_tables(meta_gs, me_exp, block, capacity):
    n_grp, n_src = meta_gs.shape[:2]
    per_block = TOK_DEV * TOP
    ids = meta_gs[..., :TOP].astype(jnp.int32).reshape(n_grp, n_src, per_block)
    wts = meta_gs[..., TOP:].astype(jnp.float32).reshape(n_grp, n_src, per_block)
    destination = ids // EXP_DEV
    local = ids % EXP_DEV
    entry = jnp.arange(per_block, dtype=jnp.int32)
    mine = destination == me_exp
    upper = (entry[:, None] < entry[None, :]).astype(jnp.bfloat16)
    rank = jnp.dot(
        mine.astype(jnp.bfloat16).reshape(-1, per_block), upper, preferred_element_type=jnp.float32
    )
    rank = rank.astype(jnp.int32).reshape(mine.shape)
    select = mine[:, :, None, :] & (
        rank[:, :, None, :] == jnp.arange(capacity, dtype=jnp.int32)[None, None, :, None]
    )
    weight = jnp.sum(jnp.where(select, wts[:, :, None, :], 0.0), axis=-1)
    label = jnp.sum(jnp.where(select, local[:, :, None, :] + 1, 0), axis=-1) - 1
    token_in_block = jnp.sum(jnp.where(select, (entry // TOP)[None, None, None, :], 0), axis=-1)
    token = token_in_block + block[:, :, None] * TOK_DEV
    return weight.reshape(-1), label.reshape(-1), token.reshape(-1)


def per_device(grad_out, combine, expert_ids, saved_hidden):
    n_exp = lax.axis_size("expert")
    n_grp = lax.axis_size("dp")
    capacity = saved_hidden.shape[3]
    width = D // n_grp
    me_exp = lax.axis_index("expert")

    meta = jnp.concatenate([expert_ids.astype(jnp.bfloat16), combine], axis=1)
    cols = jnp.transpose(grad_out.reshape(TOK_DEV, n_grp, width), (1, 0, 2))
    cols = jnp.concatenate(
        [cols, jnp.broadcast_to(meta[None], (n_grp,) + meta.shape)], axis=2
    )
    cols = lax.all_to_all(cols, "dp", 0, 0, tiled=True)

    split = n_grp // 2
    gathered = lax.all_gather(cols[split:], "expert", axis=0, tiled=False)
    hidden_src, cols = lax.optimization_barrier((saved_hidden.reshape(-1, FF), cols))
    hidden = lax.all_gather(hidden_src, "dp", axis=0, tiled=True)

    part = cols[:split]
    half = n_exp // 2
    fwd_perm = [(i, (i + 1) % n_exp) for i in range(n_exp)]
    bwd_perm = [(i, (i - 1) % n_exp) for i in range(n_exp)]
    ahead = [part]
    behind = []
    fwd = part
    bwd = part
    for step in range(1, half + 1):
        fwd = lax.ppermute(fwd, "expert", fwd_perm)
        behind.append(fwd)
        if step < n_exp - half:
            bwd = lax.ppermute(bwd, "expert", bwd_perm)
            ahead.append(bwd)
    ring = jnp.stack(ahead + behind[::-1], axis=0)
    ring_rows = ring.shape[0] * ring.shape[1] * ring.shape[2]
    tokens = jnp.concatenate(
        [ring.reshape(-1, ring.shape[-1]), gathered.reshape(-1, gathered.shape[-1])], axis=0
    )

    relative = (jnp.arange(n_exp, dtype=jnp.int32) - me_exp) % n_exp
    ring_meta = jnp.take(ring[:, :, :, width:], relative, axis=0)
    meta_src = jnp.concatenate([ring_meta, gathered[:, :, :, width:]], axis=1)
    meta_gs = jnp.transpose(meta_src, (1, 0, 2, 3))
    groups = jnp.arange(n_grp, dtype=jnp.int32)[:, None]
    sources = jnp.arange(n_exp, dtype=jnp.int32)[None, :]
    block = jnp.where(
        groups < split,
        relative[None, :] * split + groups,
        ring_rows // TOK_DEV + sources * (n_grp - split) + (groups - split),
    )
    weight, label, token = slot_tables(meta_gs, me_exp, block, capacity)

    hidden_t = jnp.transpose(hidden)
    rows_t = (weight[None, :] * hidden_t.astype(jnp.float32)).astype(jnp.bfloat16)
    grad_rows = jnp.take(tokens, token, axis=0, mode="clip")[:, :width]
    mask = label[:, None] == jnp.arange(EXP_DEV, dtype=jnp.int32)[None, :]
    spread = jnp.where(mask[:, :, None], grad_rows[:, None, :], jnp.zeros_like(grad_rows)[:, None, :])
    spread = spread.reshape(grad_rows.shape[0], EXP_DEV * width)
    gradient = jnp.dot(rows_t, spread, preferred_element_type=jnp.float32)
    gradient = gradient.astype(jnp.bfloat16).reshape(FF, EXP_DEV, width)
    return jnp.transpose(gradient, (1, 0, 2))


def solution(mesh):
    placed = (
        P(("expert", "dp"), None),
        P(("expert", "dp"), None),
        P(("expert", "dp"), None),
        P("expert", "dp", None, None, None),
    )
    return jax.shard_map(
        per_device, mesh=mesh, in_specs=placed, out_specs=P("expert", None, "dp"), check_vma=False
    )
```

```python
import jax
import jax.numpy as jnp
from jax import lax
from jax.sharding import PartitionSpec as P

D = 7168
FF = 1024
TOP = 8
EXP_DEV = 4
TOK_DEV = 8


def slot_tables(meta_gs, me_exp, relative, capacity):
    n_grp, n_src = meta_gs.shape[:2]
    per_block = TOK_DEV * TOP
    ids = meta_gs[..., :TOP].astype(jnp.int32).reshape(n_grp, n_src, per_block)
    wts = meta_gs[..., TOP:].astype(jnp.float32).reshape(n_grp, n_src, per_block)
    destination = ids // EXP_DEV
    local = ids % EXP_DEV
    entry = jnp.arange(per_block, dtype=jnp.int32)
    mine = destination == me_exp
    upper = (entry[:, None] < entry[None, :]).astype(jnp.bfloat16)
    rank = jnp.dot(
        mine.astype(jnp.bfloat16).reshape(-1, per_block), upper, preferred_element_type=jnp.float32
    )
    rank = rank.astype(jnp.int32).reshape(mine.shape)
    select = mine[:, :, None, :] & (
        rank[:, :, None, :] == jnp.arange(capacity, dtype=jnp.int32)[None, None, :, None]
    )
    weight = jnp.sum(jnp.where(select, wts[:, :, None, :], 0.0), axis=-1)
    label = jnp.sum(jnp.where(select, local[:, :, None, :] + 1, 0), axis=-1) - 1
    token_in_block = jnp.sum(jnp.where(select, (entry // TOP)[None, None, None, :], 0), axis=-1)
    block = relative[None, :] * n_grp + jnp.arange(n_grp, dtype=jnp.int32)[:, None]
    token = token_in_block + block[:, :, None] * TOK_DEV
    return weight.reshape(-1), label.reshape(-1), token.reshape(-1)


def per_device(grad_out, combine, expert_ids, saved_hidden):
    n_exp = lax.axis_size("expert")
    n_grp = lax.axis_size("dp")
    capacity = saved_hidden.shape[3]
    width = D // n_grp
    me_exp = lax.axis_index("expert")

    hidden = lax.all_gather(saved_hidden.reshape(-1, FF), "dp", axis=0, tiled=True)

    meta = jnp.concatenate([expert_ids.astype(jnp.bfloat16), combine], axis=1)
    cols = jnp.transpose(grad_out.reshape(TOK_DEV, n_grp, width), (1, 0, 2))
    cols = jnp.concatenate(
        [cols, jnp.broadcast_to(meta[None], (n_grp,) + meta.shape)], axis=2
    )
    cols = lax.all_to_all(cols, "dp", 0, 0, tiled=True)

    half = n_exp // 2
    fwd_perm = [(i, (i + 1) % n_exp) for i in range(n_exp)]
    bwd_perm = [(i, (i - 1) % n_exp) for i in range(n_exp)]
    ahead = [cols]
    behind = []
    fwd = cols
    bwd = cols
    for step in range(1, half + 1):
        fwd = lax.ppermute(fwd, "expert", fwd_perm)
        behind.append(fwd)
        if step < n_exp - half:
            bwd = lax.ppermute(bwd, "expert", bwd_perm)
            ahead.append(bwd)
    pieces = ahead + behind[::-1]
    ring = jnp.stack(pieces, axis=0)
    tokens = ring.reshape(-1, ring.shape[-1])

    relative = (jnp.arange(n_exp, dtype=jnp.int32) - me_exp) % n_exp
    meta_ring = jnp.stack([piece[:, :, width:] for piece in pieces], axis=0)
    meta_src = jnp.take(meta_ring, relative, axis=0)
    meta_gs = jnp.transpose(meta_src, (1, 0, 2, 3))
    weight, label, token = slot_tables(meta_gs, me_exp, relative, capacity)

    hidden_t = jnp.transpose(hidden)
    rows_t = (weight[None, :] * hidden_t.astype(jnp.float32)).astype(jnp.bfloat16)
    grad_rows = jnp.take(tokens, token, axis=0, mode="clip")[:, :width]
    mask = label[:, None] == jnp.arange(EXP_DEV, dtype=jnp.int32)[None, :]
    spread = jnp.where(mask[:, :, None], grad_rows[:, None, :], jnp.zeros_like(grad_rows)[:, None, :])
    spread = spread.reshape(grad_rows.shape[0], EXP_DEV * width)
    gradient = jnp.dot(rows_t, spread, preferred_element_type=jnp.float32)
    gradient = gradient.astype(jnp.bfloat16).reshape(FF, EXP_DEV, width)
    return jnp.transpose(gradient, (1, 0, 2))


def solution(mesh):
    placed = (
        P(("expert", "dp"), None),
        P(("expert", "dp"), None),
        P(("expert", "dp"), None),
        P("expert", "dp", None, None, None),
    )
    return jax.shard_map(
        per_device, mesh=mesh, in_specs=placed, out_specs=P("expert", None, "dp"), check_vma=False
    )
```

```python
import jax
import jax.numpy as jnp
from jax import lax
from jax.sharding import PartitionSpec as P

D = 7168
FF = 1024
TOP = 8
EXP_DEV = 4
TOK_DEV = 8


def slot_tables(meta_gs, me_exp, relative, capacity):
    n_grp, n_src = meta_gs.shape[:2]
    per_block = TOK_DEV * TOP
    ids = meta_gs[..., :TOP].astype(jnp.int32).reshape(n_grp, n_src, per_block)
    wts = meta_gs[..., TOP:].astype(jnp.float32).reshape(n_grp, n_src, per_block)
    destination = ids // EXP_DEV
    local = ids % EXP_DEV
    entry = jnp.arange(per_block, dtype=jnp.int32)
    mine = destination == me_exp
    upper = (entry[:, None] < entry[None, :]).astype(jnp.bfloat16)
    rank = jnp.dot(
        mine.astype(jnp.bfloat16).reshape(-1, per_block), upper, preferred_element_type=jnp.float32
    )
    rank = rank.astype(jnp.int32).reshape(mine.shape)
    select = mine[:, :, None, :] & (
        rank[:, :, None, :] == jnp.arange(capacity, dtype=jnp.int32)[None, None, :, None]
    )
    weight = jnp.sum(jnp.where(select, wts[:, :, None, :], 0.0), axis=-1)
    label = jnp.sum(jnp.where(select, local[:, :, None, :] + 1, 0), axis=-1) - 1
    token_in_block = jnp.sum(jnp.where(select, (entry // TOP)[None, None, None, :], 0), axis=-1)
    block = relative[None, :] * n_grp + jnp.arange(n_grp, dtype=jnp.int32)[:, None]
    token = token_in_block + block[:, :, None] * TOK_DEV
    return weight.reshape(-1), label.reshape(-1), token.reshape(-1)


def per_device(grad_out, combine, expert_ids, saved_hidden):
    n_exp = lax.axis_size("expert")
    n_grp = lax.axis_size("dp")
    capacity = saved_hidden.shape[3]
    width = D // n_grp
    me_exp = lax.axis_index("expert")

    hidden = lax.all_gather(saved_hidden.reshape(-1, FF), "dp", axis=0, tiled=True)

    meta = jnp.concatenate([expert_ids.astype(jnp.bfloat16), combine], axis=1)
    cols = jnp.transpose(grad_out.reshape(TOK_DEV, n_grp, width), (1, 0, 2))
    cols = jnp.concatenate(
        [cols, jnp.broadcast_to(meta[None], (n_grp,) + meta.shape)], axis=2
    )
    cols = lax.all_to_all(cols, "dp", 0, 0, tiled=True)

    half = n_exp // 2
    fwd_perm = [(i, (i + 1) % n_exp) for i in range(n_exp)]
    bwd_perm = [(i, (i - 1) % n_exp) for i in range(n_exp)]
    ahead = [cols]
    behind = []
    fwd = cols
    bwd = cols
    for step in range(1, half + 1):
        fwd = lax.ppermute(fwd, "expert", fwd_perm)
        behind.append(fwd)
        if step < n_exp - half:
            bwd = lax.ppermute(bwd, "expert", bwd_perm)
            ahead.append(bwd)
    ring = jnp.stack(ahead + behind[::-1], axis=0)
    tokens = ring.reshape(-1, ring.shape[-1])

    relative = (jnp.arange(n_exp, dtype=jnp.int32) - me_exp) % n_exp
    meta_src = jnp.take(ring[:, :, :, width:], relative, axis=0)
    meta_gs = jnp.transpose(meta_src, (1, 0, 2, 3))
    weight, label, token = slot_tables(meta_gs, me_exp, relative, capacity)

    hidden_t = jnp.transpose(hidden)
    rows_t = (weight[None, :] * hidden_t.astype(jnp.float32)).astype(jnp.bfloat16)
    back = (jnp.arange(n_exp, dtype=jnp.int32) - me_exp) % n_exp
    ring_src = jnp.take(ring[..., :width], back, axis=0)
    pick_t = (token % TOK_DEV).reshape(n_grp, n_exp, capacity)
    onehot = (pick_t[..., None] == jnp.arange(TOK_DEV, dtype=jnp.int32)).astype(jnp.bfloat16)
    grad_rows = jnp.einsum(
        "gsrt,sgtc->gsrc", onehot, ring_src, preferred_element_type=jnp.float32
    ).astype(jnp.bfloat16).reshape(-1, width)
    mask = label[:, None] == jnp.arange(EXP_DEV, dtype=jnp.int32)[None, :]
    spread = jnp.where(mask[:, :, None], grad_rows[:, None, :], jnp.zeros_like(grad_rows)[:, None, :])
    spread = spread.reshape(grad_rows.shape[0], EXP_DEV * width)
    gradient = jnp.dot(rows_t, spread, preferred_element_type=jnp.float32)
    gradient = gradient.astype(jnp.bfloat16).reshape(FF, EXP_DEV, width)
    return jnp.transpose(gradient, (1, 0, 2))


def solution(mesh):
    placed = (
        P(("expert", "dp"), None),
        P(("expert", "dp"), None),
        P(("expert", "dp"), None),
        P("expert", "dp", None, None, None),
    )
    return jax.shard_map(
        per_device, mesh=mesh, in_specs=placed, out_specs=P("expert", None, "dp"), check_vma=False
    )
```

```python
import jax
import jax.numpy as jnp
from jax import lax
from jax.sharding import PartitionSpec as P

D = 7168
FF = 1024
TOP = 8
EXP_DEV = 4
TOK_DEV = 8


def slot_tables(meta_gs, me_exp, relative, capacity):
    n_grp, n_src = meta_gs.shape[:2]
    per_block = TOK_DEV * TOP
    ids = meta_gs[..., :TOP].astype(jnp.int32).reshape(n_grp, n_src, per_block)
    wts = meta_gs[..., TOP:].astype(jnp.float32).reshape(n_grp, n_src, per_block)
    destination = ids // EXP_DEV
    local = ids % EXP_DEV
    entry = jnp.arange(per_block, dtype=jnp.int32)
    mine = destination == me_exp
    upper = (entry[:, None] < entry[None, :]).astype(jnp.bfloat16)
    rank = jnp.dot(
        mine.astype(jnp.bfloat16).reshape(-1, per_block), upper, preferred_element_type=jnp.float32
    )
    rank = rank.astype(jnp.int32).reshape(mine.shape)
    select = mine[:, :, None, :] & (
        rank[:, :, None, :] == jnp.arange(capacity, dtype=jnp.int32)[None, None, :, None]
    )
    weight = jnp.sum(jnp.where(select, wts[:, :, None, :], 0.0), axis=-1)
    label = jnp.sum(jnp.where(select, local[:, :, None, :] + 1, 0), axis=-1) - 1
    token_in_block = jnp.sum(jnp.where(select, (entry // TOP)[None, None, None, :], 0), axis=-1)
    block = relative[None, :] * n_grp + jnp.arange(n_grp, dtype=jnp.int32)[:, None]
    token = token_in_block + block[:, :, None] * TOK_DEV
    return weight.reshape(-1), label.reshape(-1), token.reshape(-1)


def per_device(grad_out, combine, expert_ids, saved_hidden):
    n_exp = lax.axis_size("expert")
    n_grp = lax.axis_size("dp")
    capacity = saved_hidden.shape[3]
    width = D // n_grp
    me_exp = lax.axis_index("expert")

    hidden = lax.all_gather(saved_hidden.reshape(-1, FF), "dp", axis=0, tiled=True)

    meta = jnp.concatenate([expert_ids.astype(jnp.bfloat16), combine], axis=1)
    cols = jnp.transpose(grad_out.reshape(TOK_DEV, n_grp, width), (1, 0, 2))
    cols = jnp.concatenate(
        [cols, jnp.broadcast_to(meta[None], (n_grp,) + meta.shape)], axis=2
    )
    cols = lax.all_to_all(cols, "dp", 0, 0, tiled=True)

    half = n_exp // 2
    fwd_perm = [(i, (i + 1) % n_exp) for i in range(n_exp)]
    bwd_perm = [(i, (i - 1) % n_exp) for i in range(n_exp)]
    ahead = [cols]
    behind = []
    fwd = cols
    bwd = cols
    for step in range(1, half + 1):
        fwd = lax.ppermute(fwd, "expert", fwd_perm)
        behind.append(fwd)
        if step < n_exp - half:
            bwd = lax.ppermute(bwd, "expert", bwd_perm)
            ahead.append(bwd)
    ring = jnp.stack(ahead + behind[::-1], axis=0)
    tokens = ring.reshape(-1, ring.shape[-1])

    relative = (jnp.arange(n_exp, dtype=jnp.int32) - me_exp) % n_exp
    meta_src = jnp.take(ring[:, :, :, width:], relative, axis=0)
    meta_gs = jnp.transpose(meta_src, (1, 0, 2, 3))
    weight, label, token = slot_tables(meta_gs, me_exp, relative, capacity)

    hidden_t = jnp.transpose(hidden)
    rows_t = (weight[None, :] * hidden_t.astype(jnp.float32)).astype(jnp.bfloat16)
    forward = (jnp.arange(n_exp, dtype=jnp.int32) + me_exp) % n_exp
    pick_t = jnp.take((token % TOK_DEV).reshape(n_grp, n_exp, capacity), forward, axis=1)
    onehot = (pick_t[..., None] == jnp.arange(TOK_DEV, dtype=jnp.int32)).astype(jnp.bfloat16)
    grad_rows = jnp.einsum(
        "gqrt,qgtc->gqrc", onehot, ring[..., :width], preferred_element_type=jnp.float32
    ).astype(jnp.bfloat16)
    grad_rows = jnp.take(grad_rows, relative, axis=1).reshape(-1, width)
    mask = label[:, None] == jnp.arange(EXP_DEV, dtype=jnp.int32)[None, :]
    spread = jnp.where(mask[:, :, None], grad_rows[:, None, :], jnp.zeros_like(grad_rows)[:, None, :])
    spread = spread.reshape(grad_rows.shape[0], EXP_DEV * width)
    gradient = jnp.dot(rows_t, spread, preferred_element_type=jnp.float32)
    gradient = gradient.astype(jnp.bfloat16).reshape(FF, EXP_DEV, width)
    return jnp.transpose(gradient, (1, 0, 2))


def solution(mesh):
    placed = (
        P(("expert", "dp"), None),
        P(("expert", "dp"), None),
        P(("expert", "dp"), None),
        P("expert", "dp", None, None, None),
    )
    return jax.shard_map(
        per_device, mesh=mesh, in_specs=placed, out_specs=P("expert", None, "dp"), check_vma=False
    )
```
